256 devices in a mesh: col: 64 (over x, z, core), row: 4 (over y).
Axes of the slice: x: 4, y: 4, z: 8, core: 2. Of those that a mesh axis runs over, the one named last changes fastest.
Arguments:
- matrix: float32 [16, 4, 256, 1, 64, 256], P(None, 'row', None, None, 'col'), as said below
Outputs:
- factored: float32 [16, 4, 256, 1, 64, 256], P(None, 'row', None, None, 'col')
Inputs may be any that keep to these rules, and one draw needn't show every extreme that they name: matrix is symmetric and positive definite, a Matern covariance of spatial sites plus a symmetric measurement term and a nugget.
All inputs are finite; a program needn't handle non-finite values.
Results may differ from the reference program's by a relative error of at most 0.0003.
Values sent between devices are 32-bit elements; how exact they have to be, the bound alone decides.
No kernel may reach another device: no remote copies, remote signals or barrier semaphores. Data moves between devices by JAX's collectives and lax.ppermute only.
A program may use at most 128 MiB of HBM per device.

```python
import math
import jax
import jax.numpy as jnp
from jax import lax

NB = 256
TC_DEV = 1
STEPS = 3
ORDER = 16384
TR_DEV = 16
N_COL = 64
N_ROW = 4


def draw_matrix(key, part):
    keys = jax.random.split(key, 2)
    index = jnp.arange(ORDER)
    jitter = jax.random.uniform(keys[0], (2, ORDER), jnp.float32, -0.4, 0.4)
    east = (index % 128).astype(jnp.float32) + jitter[0]
    north = (index // 128).astype(jnp.float32) + jitter[1]
    dist = jnp.sqrt((east[:, None] - east[None, :]) ** 2 + (north[:, None] - north[None, :]) ** 2)
    scaled = 0.57735027 * dist
    kernel = (1.0 + scaled) * jnp.exp(-scaled)
    noise = jnp.clip(0.25 * jax.random.normal(keys[1], (ORDER, ORDER), jnp.float32), -1.5, 1.5)
    symmetric = (noise + noise.T) * 0.70710678
    nugget = 0.6 * math.sqrt(ORDER) + 4.0
    full = (32.0 * kernel + symmetric + nugget * jnp.eye(ORDER, dtype=jnp.float32)) / 16.0
    return full.reshape(TR_DEV, N_ROW, NB, TC_DEV, N_COL, NB)


def setup_inputs(seed: int = 0) -> dict:
    seeds = jax.random.split(jax.random.key(seed), 2)
    return {
        "matrix": draw_matrix(jax.random.fold_in(seeds[1], 71), 0),
    }


def reference(matrix):
    full = matrix.reshape(ORDER, ORDER)
    for step in range(STEPS):
        lower_edge = step * NB
        upper_edge = lower_edge + NB
        factor = jnp.linalg.cholesky(full[lower_edge:upper_edge, lower_edge:upper_edge])
        below = full[upper_edge:, lower_edge:upper_edge]
        panel = lax.linalg.triangular_solve(factor, below, left_side=False, lower=True, transpose_a=True)
        trail_rows = ORDER - upper_edge
        count = trail_rows // NB
        rounded = panel.astype(jnp.bfloat16)
        update = jnp.dot(rounded.astype(jnp.float32), rounded.T.astype(jnp.float32), preferred_element_type=jnp.float32)
        blocks = panel.reshape(count, NB, NB)
        diag_part = jnp.einsum('tps,tqs->tpq', blocks, blocks, precision=lax.Precision.HIGHEST)
        sub_part = jnp.einsum('tps,tqs->tpq', blocks[1:], blocks[:-1], precision=lax.Precision.HIGHEST)
        grid = update.reshape(count, NB, count, NB)
        tiles_index = jnp.arange(count)
        grid = grid.at[tiles_index, :, tiles_index, :].set(diag_part)
        grid = grid.at[tiles_index[1:], :, tiles_index[:-1], :].set(sub_part)
        lower_mask = (tiles_index[:, None] >= tiles_index[None, :])[:, None, :, None]
        trail = full[upper_edge:, upper_edge:].reshape(count, NB, count, NB)
        trail = trail - jnp.where(lower_mask, grid, jnp.float32(0.0))
        full = full.at[upper_edge:, upper_edge:].set(trail.reshape(trail_rows, trail_rows))
        full = full.at[lower_edge:upper_edge, lower_edge:upper_edge].set(factor)
        full = full.at[upper_edge:, lower_edge:upper_edge].set(panel)
    return full.reshape(matrix.shape)
```

```python
import jax
import jax.numpy as jnp
from jax import lax
from jax.sharding import PartitionSpec as P

STEPS = 3
HI = lax.Precision.HIGHEST


def mm_hi(a, b):
    return jnp.einsum(
        "...ps,qs->...pq", a, b, precision=HI, preferred_element_type=jnp.float32
    )


def mm_lo(a, b):
    return jnp.einsum(
        "...ps,qs->...pq",
        a.astype(jnp.bfloat16),
        b.astype(jnp.bfloat16),
        preferred_element_type=jnp.float32,
    )


def factor(tile, eye):
    low = jnp.linalg.cholesky(tile)
    inverse = lax.linalg.triangular_solve(low, eye, left_side=True, lower=True)
    return low, inverse


def on_device(matrix):
    tile_rows = matrix.shape[0]
    width = matrix.shape[2]
    n_row = lax.axis_size("row")
    n_col = lax.axis_size("col")
    quarter = width // n_row
    my_row = lax.axis_index("row")
    my_col = lax.axis_index("col")
    tiles = matrix.reshape(tile_rows, width, width)
    eye = jnp.eye(width, dtype=jnp.float32)

    head = lax.all_gather(tiles[0], "row", axis=0, tiled=False)

    cols = lax.dynamic_slice_in_dim(head[:STEPS], my_row * quarter, quarter, axis=2)
    piece = jnp.swapaxes(cols, 1, 2)
    perm = []
    for c in range(n_col):
        for r in range(n_row):
            dst_col = c - c % n_row + r
            perm.append((c * n_row + r, dst_col * n_row + c % n_row))
    piece = lax.ppermute(piece, ("col", "row"), perm)

    gathered = lax.all_gather(piece, "col", axis=1, tiled=False)
    raw = gathered.reshape(STEPS, tile_rows, width, width)

    pick = jnp.stack(
        [
            lax.dynamic_index_in_dim(raw[:, 0], my_row % STEPS, 0, keepdims=False),
            lax.dynamic_index_in_dim(raw[:, 0], (my_row + 1) % STEPS, 0, keepdims=False),
        ]
    )
    lead = lax.all_gather(pick, "row", axis=0, tiled=False)
    a00 = lead[0, 0]
    a10 = lead[0, 1].T
    a11 = lead[1, 0]
    a21 = lead[1, 1].T
    a22 = lead[2, 0]
    a20 = lead[2, 1]

    l0, i0 = factor(a00, eye)
    p01 = mm_hi(a10, i0)
    p02 = mm_hi(a20, i0)
    b11 = a11 - mm_hi(p01, p01)
    b21 = a21 - mm_hi(p02, p01)
    b22 = a22 - mm_hi(p02, p02)
    l1, i1 = factor(b11, eye)
    p12 = mm_hi(b21, i1)
    c22 = b22 - mm_hi(p12, p12)
    l2, i2 = factor(c22, eye)

    def sub(step, target, low_rows, partner, exact_rows):
        lo = mm_lo(low_rows, partner)
        hi = mm_hi(exact_rows, partner)
        t0 = my_row
        exact = (t0 == step) | (t0 == step + 1)
        first = jnp.where(exact, hi, lo[0])
        return target - lo.at[0].set(first)

    q0 = mm_hi(raw[0], i0)
    m1 = sub(1, raw[1], q0, p01, q0[0])
    q1 = mm_hi(m1, i1)
    m2 = sub(2, raw[2], q0, p02, q0[0])
    m2 = sub(2, m2, q1, p12, q1[0])
    q2 = mm_hi(m2, i2)

    own = jnp.swapaxes(head[:STEPS], 1, 2)
    c = my_col

    def own_sub(step, target, rows, partner):
        exact = (c == step) | (c == step + 1)
        return target - jnp.where(exact, mm_hi(rows, partner), mm_lo(rows, partner))

    r0 = mm_hi(own[0], i0)
    r1 = mm_hi(own_sub(1, own[1], r0, p01), i1)
    r2 = mm_hi(own_sub(2, own_sub(2, own[2], r0, p02), r1, p12), i2)

    rows_cat = jnp.concatenate([q0, q1, q2], axis=-1)
    col_cat = jnp.concatenate([r0, r1, r2], axis=-1)
    update = mm_lo(rows_cat, col_cat)
    offset = (my_row - c) % n_row
    near = c + offset
    local = jnp.clip((near - my_row) // n_row, 0, tile_rows - 1)
    valid = (offset <= 1) & (near < tile_rows * n_row)
    exact = mm_hi(lax.dynamic_index_in_dim(rows_cat, local, 0, keepdims=False), col_cat)
    before = lax.dynamic_index_in_dim(update, local, 0, keepdims=False)
    chosen = jnp.where(valid, exact, before)
    update = lax.dynamic_update_index_in_dim(update, chosen, local, 0)

    row_ids = (jnp.arange(tile_rows, dtype=jnp.int32) * n_row + my_row)[:, None, None]
    trailing = jnp.where(row_ids >= c, tiles - update, tiles)
    panel = jnp.where(c == 0, q0, jnp.where(c == 1, q1, q2))
    diag = jnp.where(c == 0, l0, jnp.where(c == 1, l1, l2))
    leading = jnp.where(row_ids > c, panel, jnp.where(row_ids == c, diag[None], tiles))
    out = jnp.where(c >= STEPS, trailing, leading)
    return out.reshape(matrix.shape)


def solution(mesh):
    placed = (P(None, "row", None, None, "col", None),)
    return jax.shard_map(
        on_device,
        mesh=mesh,
        in_specs=placed,
        out_specs=P(None, "row", None, None, "col", None),
        check_vma=False,
    )
```

```python
import jax
import jax.numpy as jnp
from jax import lax
from jax.sharding import PartitionSpec as P

STEPS = 3
HI = lax.Precision.HIGHEST


def mm_hi(a, b):
    return jnp.einsum(
        "...ps,qs->...pq", a, b, precision=HI, preferred_element_type=jnp.float32
    )


def mm_lo(a, b):
    return jnp.einsum(
        "...ps,qs->...pq",
        a.astype(jnp.bfloat16),
        b.astype(jnp.bfloat16),
        preferred_element_type=jnp.float32,
    )


def factor(tile, eye):
    low = jnp.linalg.cholesky(tile)
    inverse = lax.linalg.triangular_solve(low, eye, left_side=True, lower=True)
    return low, inverse


def on_device(matrix):
    tile_rows = matrix.shape[0]
    width = matrix.shape[2]
    n_row = lax.axis_size("row")
    n_col = lax.axis_size("col")
    quarter = width // n_row
    my_row = lax.axis_index("row")
    my_col = lax.axis_index("col")
    tiles = matrix.reshape(tile_rows, width, width)
    eye = jnp.eye(width, dtype=jnp.float32)

    head = lax.all_gather(tiles[0], "row", axis=0, tiled=False)

    cols = lax.dynamic_slice_in_dim(head[:STEPS], my_row * quarter, quarter, axis=2)
    piece = jnp.swapaxes(cols, 1, 2)
    perm = []
    for c in range(n_col):
        for r in range(n_row):
            dst_col = c - c % n_row + r
            perm.append((c * n_row + r, dst_col * n_row + c % n_row))
    piece = lax.ppermute(piece, ("col", "row"), perm)

    gathered = lax.all_gather(piece, "col", axis=1, tiled=False)
    raw = gathered.reshape(STEPS, tile_rows, width, width)

    source = [(my_row + k) % STEPS for k in range(2)]
    share = jnp.stack([jnp.where(my_col == s, tiles[0], 0.0) for s in source])
    span = 1
    while span < n_col:
        moved = lax.ppermute(share, "col", [(i, (i + span) % n_col) for i in range(n_col)])
        held = jnp.stack([(my_col - s) % n_col < span for s in source])
        share = jnp.where(held[:, None, None], share, moved)
        span *= 2
    shares = [share] + [
        lax.ppermute(share, "row", [(i, (i + d) % n_row) for i in range(n_row)])
        for d in range(1, n_row)
    ]
    shares = jnp.stack(shares)

    def lead(group, k):
        from_group = lax.dynamic_index_in_dim(shares, (my_row - group) % n_row, 0, keepdims=False)
        return from_group[k]

    a00 = lead(0, 0)
    a10 = lead(0, 1).T
    a11 = lead(1, 0)
    a21 = lead(1, 1).T
    a22 = lead(2, 0)
    a20 = lead(2, 1)

    l0, i0 = factor(a00, eye)
    p01 = mm_hi(a10, i0)
    p02 = mm_hi(a20, i0)
    b11 = a11 - mm_hi(p01, p01)
    b21 = a21 - mm_hi(p02, p01)
    b22 = a22 - mm_hi(p02, p02)
    l1, i1 = factor(b11, eye)
    p12 = mm_hi(b21, i1)
    c22 = b22 - mm_hi(p12, p12)
    l2, i2 = factor(c22, eye)

    def sub(step, target, low_rows, partner, exact_rows):
        lo = mm_lo(low_rows, partner)
        hi = mm_hi(exact_rows, partner)
        t0 = my_row
        exact = (t0 == step) | (t0 == step + 1)
        first = jnp.where(exact, hi, lo[0])
        return target - lo.at[0].set(first)

    q0 = mm_hi(raw[0], i0)
    m1 = sub(1, raw[1], q0, p01, q0[0])
    q1 = mm_hi(m1, i1)
    m2 = sub(2, raw[2], q0, p02, q0[0])
    m2 = sub(2, m2, q1, p12, q1[0])
    q2 = mm_hi(m2, i2)

    own = jnp.swapaxes(head[:STEPS], 1, 2)
    c = my_col

    def own_sub(step, target, rows, partner):
        exact = (c == step) | (c == step + 1)
        return target - jnp.where(exact, mm_hi(rows, partner), mm_lo(rows, partner))

    r0 = mm_hi(own[0], i0)
    r1 = mm_hi(own_sub(1, own[1], r0, p01), i1)
    r2 = mm_hi(own_sub(2, own_sub(2, own[2], r0, p02), r1, p12), i2)

    rows_cat = jnp.concatenate([q0, q1, q2], axis=-1)
    col_cat = jnp.concatenate([r0, r1, r2], axis=-1)
    update = mm_lo(rows_cat, col_cat)
    offset = (my_row - c) % n_row
    near = c + offset
    local = jnp.clip((near - my_row) // n_row, 0, tile_rows - 1)
    valid = (offset <= 1) & (near < tile_rows * n_row)
    exact = mm_hi(lax.dynamic_index_in_dim(rows_cat, local, 0, keepdims=False), col_cat)
    before = lax.dynamic_index_in_dim(update, local, 0, keepdims=False)
    chosen = jnp.where(valid, exact, before)
    update = lax.dynamic_update_index_in_dim(update, chosen, local, 0)

    row_ids = (jnp.arange(tile_rows, dtype=jnp.int32) * n_row + my_row)[:, None, None]
    trailing = jnp.where(row_ids >= c, tiles - update, tiles)
    panel = jnp.where(c == 0, q0, jnp.where(c == 1, q1, q2))
    diag = jnp.where(c == 0, l0, jnp.where(c == 1, l1, l2))
    leading = jnp.where(row_ids > c, panel, jnp.where(row_ids == c, diag[None], tiles))
    out = jnp.where(c >= STEPS, trailing, leading)
    return out.reshape(matrix.shape)


def solution(mesh):
    placed = (P(None, "row", None, None, "col", None),)
    return jax.shard_map(
        on_device,
        mesh=mesh,
        in_specs=placed,
        out_specs=P(None, "row", None, None, "col", None),
        check_vma=False,
    )
```

```python
import jax
import jax.numpy as jnp
from jax import lax
from jax.sharding import PartitionSpec as P

STEPS = 3
HI = lax.Precision.HIGHEST


def mm_hi(a, b):
    return jnp.einsum(
        "...ps,qs->...pq", a, b, precision=HI, preferred_element_type=jnp.float32
    )


def mm_lo(a, b):
    return jnp.einsum(
        "...ps,qs->...pq",
        a.astype(jnp.bfloat16),
        b.astype(jnp.bfloat16),
        preferred_element_type=jnp.float32,
    )


def factor(tile, eye):
    low = jnp.linalg.cholesky(tile)
    inverse = lax.linalg.triangular_solve(low, eye, left_side=True, lower=True)
    return low, inverse


def on_device(matrix):
    tile_rows = matrix.shape[0]
    width = matrix.shape[2]
    n_row = lax.axis_size("row")
    n_col = lax.axis_size("col")
    quarter = width // n_row
    my_row = lax.axis_index("row")
    my_col = lax.axis_index("col")
    tiles = matrix.reshape(tile_rows, width, width)
    eye = jnp.eye(width, dtype=jnp.float32)

    head = lax.all_gather(tiles[0], "row", axis=0, tiled=False)

    source = [(my_row + k) % STEPS for k in range(2)]
    share = jnp.stack([jnp.where(my_col == s, tiles[0], 0.0) for s in source])
    span = 1
    while span < n_col:
        moved = lax.ppermute(share, "col", [(i, (i + span) % n_col) for i in range(n_col)])
        held = jnp.stack([(my_col - s) % n_col < span for s in source])
        share = jnp.where(held[:, None, None], share, moved)
        span *= 2
    shares = [share] + [
        lax.ppermute(share, "row", [(i, (i + d) % n_row) for i in range(n_row)])
        for d in range(1, n_row)
    ]
    shares = jnp.stack(shares)

    cols = lax.dynamic_slice_in_dim(head[:STEPS], my_row * quarter, quarter, axis=2)
    piece = jnp.swapaxes(cols, 1, 2)
    perm = []
    for c in range(n_col):
        for r in range(n_row):
            dst_col = c - c % n_row + r
            perm.append((c * n_row + r, dst_col * n_row + c % n_row))
    piece, shares = lax.optimization_barrier((piece, shares))
    piece = lax.ppermute(piece, ("col", "row"), perm)

    gathered = lax.all_gather(piece, "col", axis=1, tiled=False)
    raw = gathered.reshape(STEPS, tile_rows, width, width)

    def lead(group, k):
        from_group = lax.dynamic_index_in_dim(shares, (my_row - group) % n_row, 0, keepdims=False)
        return from_group[k]

    a00 = lead(0, 0)
    a10 = lead(0, 1).T
    a11 = lead(1, 0)
    a21 = lead(1, 1).T
    a22 = lead(2, 0)
    a20 = lead(2, 1)

    l0, i0 = factor(a00, eye)
    p01 = mm_hi(a10, i0)
    p02 = mm_hi(a20, i0)
    b11 = a11 - mm_hi(p01, p01)
    b21 = a21 - mm_hi(p02, p01)
    b22 = a22 - mm_hi(p02, p02)
    l1, i1 = factor(b11, eye)
    p12 = mm_hi(b21, i1)
    c22 = b22 - mm_hi(p12, p12)
    l2, i2 = factor(c22, eye)

    def sub(step, target, low_rows, partner, exact_rows):
        lo = mm_lo(low_rows, partner)
        hi = mm_hi(exact_rows, partner)
        t0 = my_row
        exact = (t0 == step) | (t0 == step + 1)
        first = jnp.where(exact, hi, lo[0])
        return target - lo.at[0].set(first)

    q0 = mm_hi(raw[0], i0)
    m1 = sub(1, raw[1], q0, p01, q0[0])
    q1 = mm_hi(m1, i1)
    m2 = sub(2, raw[2], q0, p02, q0[0])
    m2 = sub(2, m2, q1, p12, q1[0])
    q2 = mm_hi(m2, i2)

    own = jnp.swapaxes(head[:STEPS], 1, 2)
    c = my_col

    def own_sub(step, target, rows, partner):
        exact = (c == step) | (c == step + 1)
        return target - jnp.where(exact, mm_hi(rows, partner), mm_lo(rows, partner))

    r0 = mm_hi(own[0], i0)
    r1 = mm_hi(own_sub(1, own[1], r0, p01), i1)
    r2 = mm_hi(own_sub(2, own_sub(2, own[2], r0, p02), r1, p12), i2)

    rows_cat = jnp.concatenate([q0, q1, q2], axis=-1)
    col_cat = jnp.concatenate([r0, r1, r2], axis=-1)
    update = mm_lo(rows_cat, col_cat)
    offset = (my_row - c) % n_row
    near = c + offset
    local = jnp.clip((near - my_row) // n_row, 0, tile_rows - 1)
    valid = (offset <= 1) & (near < tile_rows * n_row)
    exact = mm_hi(lax.dynamic_index_in_dim(rows_cat, local, 0, keepdims=False), col_cat)
    before = lax.dynamic_index_in_dim(update, local, 0, keepdims=False)
    chosen = jnp.where(valid, exact, before)
    update = lax.dynamic_update_index_in_dim(update, chosen, local, 0)

    row_ids = (jnp.arange(tile_rows, dtype=jnp.int32) * n_row + my_row)[:, None, None]
    trailing = jnp.where(row_ids >= c, tiles - update, tiles)
    panel = jnp.where(c == 0, q0, jnp.where(c == 1, q1, q2))
    diag = jnp.where(c == 0, l0, jnp.where(c == 1, l1, l2))
    leading = jnp.where(row_ids > c, panel, jnp.where(row_ids == c, diag[None], tiles))
    out = jnp.where(c >= STEPS, trailing, leading)
    return out.reshape(matrix.shape)


def solution(mesh):
    placed = (P(None, "row", None, None, "col", None),)
    return jax.shard_map(
        on_device,
        mesh=mesh,
        in_specs=placed,
        out_specs=P(None, "row", None, None, "col", None),
        check_vma=False,
    )
```

```python
import jax
import jax.numpy as jnp
from jax import lax
from jax.sharding import PartitionSpec as P

STEPS = 3
HI = lax.Precision.HIGHEST


def mm_hi(a, b):
    return jnp.einsum(
        "...ps,qs->...pq", a, b, precision=HI, preferred_element_type=jnp.float32
    )


def mm_lo(a, b):
    return jnp.einsum(
        "...ps,qs->...pq",
        a.astype(jnp.bfloat16),
        b.astype(jnp.bfloat16),
        preferred_element_type=jnp.float32,
    )


def factor(tile, eye):
    low = jnp.linalg.cholesky(tile)
    inverse = lax.linalg.triangular_solve(low, eye, left_side=True, lower=True)
    return low, inverse


def on_device(matrix):
    tile_rows = matrix.shape[0]
    width = matrix.shape[2]
    n_row = lax.axis_size("row")
    n_col = lax.axis_size("col")
    quarter = width // n_row
    my_row = lax.axis_index("row")
    my_col = lax.axis_index("col")
    tiles = matrix.reshape(tile_rows, width, width)
    eye = jnp.eye(width, dtype=jnp.float32)

    head = lax.all_gather(tiles[0], "row", axis=0, tiled=False)

    slots = []
    for i in range(STEPS):
        for j in range(i + 1):
            slots.append(jnp.where((my_row == i) & (my_col == j), tiles[0], 0.0))
    block = lax.psum(jnp.stack(slots), ("col", "row"))

    cols = lax.dynamic_slice_in_dim(head[:STEPS], my_row * quarter, quarter, axis=2)
    piece = jnp.swapaxes(cols, 1, 2)
    perm = []
    for c in range(n_col):
        for r in range(n_row):
            dst_col = c - c % n_row + r
            perm.append((c * n_row + r, dst_col * n_row + c % n_row))
    piece, block = lax.optimization_barrier((piece, block))
    piece = lax.ppermute(piece, ("col", "row"), perm)

    gathered = lax.all_gather(piece, "col", axis=1, tiled=False)
    raw = gathered.reshape(STEPS, tile_rows, width, width)

    a00, a10, a11, a20, a21, a22 = [block[k] for k in range(6)]

    l0, i0 = factor(a00, eye)
    p01 = mm_hi(a10, i0)
    p02 = mm_hi(a20, i0)
    b11 = a11 - mm_hi(p01, p01)
    b21 = a21 - mm_hi(p02, p01)
    b22 = a22 - mm_hi(p02, p02)
    l1, i1 = factor(b11, eye)
    p12 = mm_hi(b21, i1)
    c22 = b22 - mm_hi(p12, p12)
    l2, i2 = factor(c22, eye)

    def sub(step, target, low_rows, partner, exact_rows):
        lo = mm_lo(low_rows, partner)
        hi = mm_hi(exact_rows, partner)
        t0 = my_row
        exact = (t0 == step) | (t0 == step + 1)
        first = jnp.where(exact, hi, lo[0])
        return target - lo.at[0].set(first)

    q0 = mm_hi(raw[0], i0)
    m1 = sub(1, raw[1], q0, p01, q0[0])
    q1 = mm_hi(m1, i1)
    m2 = sub(2, raw[2], q0, p02, q0[0])
    m2 = sub(2, m2, q1, p12, q1[0])
    q2 = mm_hi(m2, i2)

    own = jnp.swapaxes(head[:STEPS], 1, 2)
    c = my_col

    def own_sub(step, target, rows, partner):
        exact = (c == step) | (c == step + 1)
        return target - jnp.where(exact, mm_hi(rows, partner), mm_lo(rows, partner))

    r0 = mm_hi(own[0], i0)
    r1 = mm_hi(own_sub(1, own[1], r0, p01), i1)
    r2 = mm_hi(own_sub(2, own_sub(2, own[2], r0, p02), r1, p12), i2)

    rows_cat = jnp.concatenate([q0, q1, q2], axis=-1)
    col_cat = jnp.concatenate([r0, r1, r2], axis=-1)
    update = mm_lo(rows_cat, col_cat)
    offset = (my_row - c) % n_row
    near = c + offset
    local = jnp.clip((near - my_row) // n_row, 0, tile_rows - 1)
    valid = (offset <= 1) & (near < tile_rows * n_row)
    exact = mm_hi(lax.dynamic_index_in_dim(rows_cat, local, 0, keepdims=False), col_cat)
    before = lax.dynamic_index_in_dim(update, local, 0, keepdims=False)
    chosen = jnp.where(valid, exact, before)
    update = lax.dynamic_update_index_in_dim(update, chosen, local, 0)

    row_ids = (jnp.arange(tile_rows, dtype=jnp.int32) * n_row + my_row)[:, None, None]
    trailing = jnp.where(row_ids >= c, tiles - update, tiles)
    panel = jnp.where(c == 0, q0, jnp.where(c == 1, q1, q2))
    diag = jnp.where(c == 0, l0, jnp.where(c == 1, l1, l2))
    leading = jnp.where(row_ids > c, panel, jnp.where(row_ids == c, diag[None], tiles))
    out = jnp.where(c >= STEPS, trailing, leading)
    return out.reshape(matrix.shape)


def solution(mesh):
    placed = (P(None, "row", None, None, "col", None),)
    return jax.shard_map(
        on_device,
        mesh=mesh,
        in_specs=placed,
        out_specs=P(None, "row", None, None, "col", None),
        check_vma=False,
    )
```

```python
import jax
import jax.numpy as jnp
from jax import lax
from jax.sharding import PartitionSpec as P

STEPS = 3
HI = lax.Precision.HIGHEST


def mm_hi(a, b):
    return jnp.einsum(
        "...ps,qs->...pq", a, b, precision=HI, preferred_element_type=jnp.float32
    )


def mm_lo(a, b):
    return jnp.einsum(
        "...ps,qs->...pq",
        a.astype(jnp.bfloat16),
        b.astype(jnp.bfloat16),
        preferred_element_type=jnp.float32,
    )


def factor(tile, eye):
    half = tile.shape[0] // 2
    unit = eye[:half, :half]
    la = jnp.linalg.cholesky(tile[:half, :half])
    ia = lax.linalg.triangular_solve(la, unit, left_side=True, lower=True)
    lb = mm_hi(tile[half:, :half], ia)
    lc = jnp.linalg.cholesky(tile[half:, half:] - mm_hi(lb, lb))
    ic = lax.linalg.triangular_solve(lc, unit, left_side=True, lower=True)
    corner = -jnp.matmul(ic, jnp.matmul(lb, ia, precision=HI), precision=HI)
    zero = jnp.zeros_like(unit)
    low = jnp.block([[la, zero], [lb, lc]])
    inverse = jnp.block([[ia, zero], [corner, ic]])
    return low, inverse


def on_device(matrix):
    tile_rows = matrix.shape[0]
    width = matrix.shape[2]
    n_row = lax.axis_size("row")
    n_col = lax.axis_size("col")
    quarter = width // n_row
    my_row = lax.axis_index("row")
    my_col = lax.axis_index("col")
    tiles = matrix.reshape(tile_rows, width, width)
    eye = jnp.eye(width, dtype=jnp.float32)

    head = lax.all_gather(tiles[0], "row", axis=0, tiled=False)

    cols = lax.dynamic_slice_in_dim(head[:STEPS], my_row * quarter, quarter, axis=2)
    piece = jnp.swapaxes(cols, 1, 2)
    perm = []
    for c in range(n_col):
        for r in range(n_row):
            dst_col = c - c % n_row + r
            perm.append((c * n_row + r, dst_col * n_row + c % n_row))
    piece = lax.ppermute(piece, ("col", "row"), perm)

    gathered = lax.all_gather(piece, "col", axis=1, tiled=False)
    raw = gathered.reshape(STEPS, tile_rows, width, width)

    pick = jnp.stack(
        [
            lax.dynamic_index_in_dim(raw[:, 0], my_row % STEPS, 0, keepdims=False),
            lax.dynamic_index_in_dim(raw[:, 0], (my_row + 1) % STEPS, 0, keepdims=False),
        ]
    )
    lead = lax.all_gather(pick, "row", axis=0, tiled=False)
    a00 = lead[0, 0]
    a10 = lead[0, 1].T
    a11 = lead[1, 0]
    a21 = lead[1, 1].T
    a22 = lead[2, 0]
    a20 = lead[2, 1]

    l0, i0 = factor(a00, eye)
    p01 = mm_hi(a10, i0)
    p02 = mm_hi(a20, i0)
    b11 = a11 - mm_hi(p01, p01)
    b21 = a21 - mm_hi(p02, p01)
    b22 = a22 - mm_hi(p02, p02)
    l1, i1 = factor(b11, eye)
    p12 = mm_hi(b21, i1)
    c22 = b22 - mm_hi(p12, p12)
    l2, i2 = factor(c22, eye)

    def sub(step, target, low_rows, partner, exact_rows):
        lo = mm_lo(low_rows, partner)
        hi = mm_hi(exact_rows, partner)
        t0 = my_row
        exact = (t0 == step) | (t0 == step + 1)
        first = jnp.where(exact, hi, lo[0])
        return target - lo.at[0].set(first)

    q0 = mm_hi(raw[0], i0)
    m1 = sub(1, raw[1], q0, p01, q0[0])
    q1 = mm_hi(m1, i1)
    m2 = sub(2, raw[2], q0, p02, q0[0])
    m2 = sub(2, m2, q1, p12, q1[0])
    q2 = mm_hi(m2, i2)

    own = jnp.swapaxes(head[:STEPS], 1, 2)
    c = my_col

    def own_sub(step, target, rows, partner):
        exact = (c == step) | (c == step + 1)
        return target - jnp.where(exact, mm_hi(rows, partner), mm_lo(rows, partner))

    r0 = mm_hi(own[0], i0)
    r1 = mm_hi(own_sub(1, own[1], r0, p01), i1)
    r2 = mm_hi(own_sub(2, own_sub(2, own[2], r0, p02), r1, p12), i2)

    update = mm_lo(q0, r0) + mm_lo(q1, r1) + mm_lo(q2, r2)
    offset = (my_row - c) % n_row
    near = c + offset
    local = jnp.clip((near - my_row) // n_row, 0, tile_rows - 1)
    valid = (offset <= 1) & (near < tile_rows * n_row)

    def row_of(q):
        return lax.dynamic_index_in_dim(q, local, 0, keepdims=False)

    exact = mm_hi(row_of(q0), r0) + mm_hi(row_of(q1), r1) + mm_hi(row_of(q2), r2)
    before = lax.dynamic_index_in_dim(update, local, 0, keepdims=False)
    chosen = jnp.where(valid, exact, before)
    update = lax.dynamic_update_index_in_dim(update, chosen, local, 0)

    row_ids = (jnp.arange(tile_rows, dtype=jnp.int32) * n_row + my_row)[:, None, None]
    trailing = jnp.where(row_ids >= c, tiles - update, tiles)
    panel = jnp.where(c == 0, q0, jnp.where(c == 1, q1, q2))
    diag = jnp.where(c == 0, l0, jnp.where(c == 1, l1, l2))
    leading = jnp.where(row_ids > c, panel, jnp.where(row_ids == c, diag[None], tiles))
    out = jnp.where(c >= STEPS, trailing, leading)
    return out.reshape(matrix.shape)


def solution(mesh):
    placed = (P(None, "row", None, None, "col", None),)
    return jax.shard_map(
        on_device,
        mesh=mesh,
        in_specs=placed,
        out_specs=P(None, "row", None, None, "col", None),
        check_vma=False,
    )
```

```python
import jax
import jax.numpy as jnp
from jax import lax
from jax.sharding import PartitionSpec as P

STEPS = 3
HI = lax.Precision.HIGHEST


def mm_hi(a, b):
    return jnp.einsum(
        "...ps,qs->...pq", a, b, precision=HI, preferred_element_type=jnp.float32
    )


def mm_lo(a, b):
    return jnp.einsum(
        "...ps,qs->...pq",
        a.astype(jnp.bfloat16),
        b.astype(jnp.bfloat16),
        preferred_element_type=jnp.float32,
    )


def factor(tile, eye):
    half = tile.shape[0] // 2
    unit = eye[:half, :half]
    la = jnp.linalg.cholesky(tile[:half, :half])
    ia = lax.linalg.triangular_solve(la, unit, left_side=True, lower=True)
    lb = mm_hi(tile[half:, :half], ia)
    lc = jnp.linalg.cholesky(tile[half:, half:] - mm_hi(lb, lb))
    ic = lax.linalg.triangular_solve(lc, unit, left_side=True, lower=True)
    corner = -jnp.matmul(ic, jnp.matmul(lb, ia, precision=HI), precision=HI)
    zero = jnp.zeros_like(unit)
    low = jnp.block([[la, zero], [lb, lc]])
    inverse = jnp.block([[ia, zero], [corner, ic]])
    return low, inverse


def on_device(matrix):
    tile_rows = matrix.shape[0]
    width = matrix.shape[2]
    n_row = lax.axis_size("row")
    n_col = lax.axis_size("col")
    quarter = width // n_row
    my_row = lax.axis_index("row")
    my_col = lax.axis_index("col")
    tiles = matrix.reshape(tile_rows, width, width)
    eye = jnp.eye(width, dtype=jnp.float32)

    head = lax.all_gather(tiles[0], "row", axis=0, tiled=False)

    chunk = STEPS * width * width // n_col
    chunks = lax.all_to_all(
        head[:STEPS].reshape(n_col, chunk), "col", 0, 0, tiled=True
    )
    lead = lax.all_gather(chunks[:STEPS], "col", axis=0, tiled=False)

    cols = lax.dynamic_slice_in_dim(head[:STEPS], my_row * quarter, quarter, axis=2)
    piece = jnp.swapaxes(cols, 1, 2)
    perm = []
    for c in range(n_col):
        for r in range(n_row):
            dst_col = c - c % n_row + r
            perm.append((c * n_row + r, dst_col * n_row + c % n_row))
    piece, lead = lax.optimization_barrier((piece, lead))
    piece = lax.ppermute(piece, ("col", "row"), perm)

    gathered = lax.all_gather(piece, "col", axis=1, tiled=False)
    raw = gathered.reshape(STEPS, tile_rows, width, width)

    block = [lead[:, j].reshape(STEPS, width, width) for j in range(STEPS)]
    a00 = block[0][0]
    a10 = block[0][1]
    a20 = block[0][2]
    a11 = block[1][1]
    a21 = block[1][2]
    a22 = block[2][2]

    l0, i0 = factor(a00, eye)
    p01 = mm_hi(a10, i0)
    p02 = mm_hi(a20, i0)
    b11 = a11 - mm_hi(p01, p01)
    b21 = a21 - mm_hi(p02, p01)
    b22 = a22 - mm_hi(p02, p02)
    l1, i1 = factor(b11, eye)
    p12 = mm_hi(b21, i1)
    c22 = b22 - mm_hi(p12, p12)
    l2, i2 = factor(c22, eye)

    def sub(step, target, low_rows, partner, exact_rows):
        lo = mm_lo(low_rows, partner)
        hi = mm_hi(exact_rows, partner)
        t0 = my_row
        exact = (t0 == step) | (t0 == step + 1)
        first = jnp.where(exact, hi, lo[0])
        return target - lo.at[0].set(first)

    q0 = mm_hi(raw[0], i0)
    m1 = sub(1, raw[1], q0, p01, q0[0])
    q1 = mm_hi(m1, i1)
    m2 = sub(2, raw[2], q0, p02, q0[0])
    m2 = sub(2, m2, q1, p12, q1[0])
    q2 = mm_hi(m2, i2)

    own = jnp.swapaxes(head[:STEPS], 1, 2)
    c = my_col

    def own_sub(step, target, rows, partner):
        exact = (c == step) | (c == step + 1)
        return target - jnp.where(exact, mm_hi(rows, partner), mm_lo(rows, partner))

    r0 = mm_hi(own[0], i0)
    r1 = mm_hi(own_sub(1, own[1], r0, p01), i1)
    r2 = mm_hi(own_sub(2, own_sub(2, own[2], r0, p02), r1, p12), i2)

    update = mm_lo(q0, r0) + mm_lo(q1, r1) + mm_lo(q2, r2)
    offset = (my_row - c) % n_row
    near = c + offset
    local = jnp.clip((near - my_row) // n_row, 0, tile_rows - 1)
    valid = (offset <= 1) & (near < tile_rows * n_row)

    def row_of(q):
        return lax.dynamic_index_in_dim(q, local, 0, keepdims=False)

    exact = mm_hi(row_of(q0), r0) + mm_hi(row_of(q1), r1) + mm_hi(row_of(q2), r2)
    before = lax.dynamic_index_in_dim(update, local, 0, keepdims=False)
    chosen = jnp.where(valid, exact, before)
    update = lax.dynamic_update_index_in_dim(update, chosen, local, 0)

    row_ids = (jnp.arange(tile_rows, dtype=jnp.int32) * n_row + my_row)[:, None, None]
    trailing = jnp.where(row_ids >= c, tiles - update, tiles)
    panel = jnp.where(c == 0, q0, jnp.where(c == 1, q1, q2))
    diag = jnp.where(c == 0, l0, jnp.where(c == 1, l1, l2))
    leading = jnp.where(row_ids > c, panel, jnp.where(row_ids == c, diag[None], tiles))
    out = jnp.where(c >= STEPS, trailing, leading)
    return out.reshape(matrix.shape)


def solution(mesh):
    placed = (P(None, "row", None, None, "col", None),)
    return jax.shard_map(
        on_device,
        mesh=mesh,
        in_specs=placed,
        out_specs=P(None, "row", None, None, "col", None),
        check_vma=False,
    )
```

```python
import jax
import jax.numpy as jnp
from jax import lax
from jax.sharding import PartitionSpec as P

STEPS = 3
HI = lax.Precision.HIGHEST


def mm_hi(a, b):
    return jnp.einsum(
        "...ps,qs->...pq", a, b, precision=HI, preferred_element_type=jnp.float32
    )


def mm_lo(a, b):
    return jnp.einsum(
        "...ps,qs->...pq",
        a.astype(jnp.bfloat16),
        b.astype(jnp.bfloat16),
        preferred_element_type=jnp.float32,
    )


def factor(tile, eye):
    half = tile.shape[0] // 2
    unit = eye[:half, :half]
    la = jnp.linalg.cholesky(tile[:half, :half])
    ia = lax.linalg.triangular_solve(la, unit, left_side=True, lower=True)
    lb = mm_hi(tile[half:, :half], ia)
    lc = jnp.linalg.cholesky(tile[half:, half:] - mm_hi(lb, lb))
    ic = lax.linalg.triangular_solve(lc, unit, left_side=True, lower=True)
    corner = -jnp.matmul(ic, jnp.matmul(lb, ia, precision=HI), precision=HI)
    zero = jnp.zeros_like(unit)
    low = jnp.block([[la, zero], [lb, lc]])
    inverse = jnp.block([[ia, zero], [corner, ic]])
    return low, inverse


def on_device(matrix):
    tile_rows = matrix.shape[0]
    width = matrix.shape[2]
    n_row = lax.axis_size("row")
    n_col = lax.axis_size("col")
    quarter = width // n_row
    my_row = lax.axis_index("row")
    my_col = lax.axis_index("col")
    tiles = matrix.reshape(tile_rows, width, width)
    eye = jnp.eye(width, dtype=jnp.float32)

    head = lax.all_gather(tiles[0], "row", axis=0, tiled=False)

    rows = n_row * width // n_col
    chunks = lax.all_to_all(
        head.reshape(n_col, rows, width), "col", 0, 0, tiled=True
    )
    lead = lax.all_gather(chunks[:STEPS], "col", axis=0, tiled=True)

    cols = lax.dynamic_slice_in_dim(head[:STEPS], my_row * quarter, quarter, axis=2)
    piece = jnp.swapaxes(cols, 1, 2)
    perm = []
    for c in range(n_col):
        for r in range(n_row):
            dst_col = c - c % n_row + r
            perm.append((c * n_row + r, dst_col * n_row + c % n_row))
    piece, lead = lax.optimization_barrier((piece, lead))
    piece = lax.ppermute(piece, ("col", "row"), perm)

    gathered = lax.all_gather(piece, "col", axis=1, tiled=False)
    raw = gathered.reshape(STEPS, tile_rows, width, width)

    lead = lead.reshape(n_col, STEPS, rows, width)
    block = [lead[:, j].reshape(n_row, width, width) for j in range(STEPS)]
    a00 = block[0][0]
    a10 = block[0][1]
    a20 = block[0][2]
    a11 = block[1][1]
    a21 = block[1][2]
    a22 = block[2][2]

    l0, i0 = factor(a00, eye)
    p01 = mm_hi(a10, i0)
    p02 = mm_hi(a20, i0)
    b11 = a11 - mm_hi(p01, p01)
    b21 = a21 - mm_hi(p02, p01)
    b22 = a22 - mm_hi(p02, p02)
    l1, i1 = factor(b11, eye)
    p12 = mm_hi(b21, i1)
    c22 = b22 - mm_hi(p12, p12)
    l2, i2 = factor(c22, eye)

    def sub(step, target, low_rows, partner, exact_rows):
        lo = mm_lo(low_rows, partner)
        hi = mm_hi(exact_rows, partner)
        t0 = my_row
        exact = (t0 == step) | (t0 == step + 1)
        first = jnp.where(exact, hi, lo[0])
        return target - lo.at[0].set(first)

    q0 = mm_hi(raw[0], i0)
    m1 = sub(1, raw[1], q0, p01, q0[0])
    q1 = mm_hi(m1, i1)
    m2 = sub(2, raw[2], q0, p02, q0[0])
    m2 = sub(2, m2, q1, p12, q1[0])
    q2 = mm_hi(m2, i2)

    own = jnp.swapaxes(head[:STEPS], 1, 2)
    c = my_col

    def own_sub(step, target, rows, partner):
        exact = (c == step) | (c == step + 1)
        return target - jnp.where(exact, mm_hi(rows, partner), mm_lo(rows, partner))

    r0 = mm_hi(own[0], i0)
    r1 = mm_hi(own_sub(1, own[1], r0, p01), i1)
    r2 = mm_hi(own_sub(2, own_sub(2, own[2], r0, p02), r1, p12), i2)

    update = mm_lo(q0, r0) + mm_lo(q1, r1) + mm_lo(q2, r2)
    offset = (my_row - c) % n_row
    near = c + offset
    local = jnp.clip((near - my_row) // n_row, 0, tile_rows - 1)
    valid = (offset <= 1) & (near < tile_rows * n_row)

    def row_of(q):
        return lax.dynamic_index_in_dim(q, local, 0, keepdims=False)

    exact = mm_hi(row_of(q0), r0) + mm_hi(row_of(q1), r1) + mm_hi(row_of(q2), r2)
    before = lax.dynamic_index_in_dim(update, local, 0, keepdims=False)
    chosen = jnp.where(valid, exact, before)
    update = lax.dynamic_update_index_in_dim(update, chosen, local, 0)

    row_ids = (jnp.arange(tile_rows, dtype=jnp.int32) * n_row + my_row)[:, None, None]
    trailing = jnp.where(row_ids >= c, tiles - update, tiles)
    panel = jnp.where(c == 0, q0, jnp.where(c == 1, q1, q2))
    diag = jnp.where(c == 0, l0, jnp.where(c == 1, l1, l2))
    leading = jnp.where(row_ids > c, panel, jnp.where(row_ids == c, diag[None], tiles))
    out = jnp.where(c >= STEPS, trailing, leading)
    return out.reshape(matrix.shape)


def solution(mesh):
    placed = (P(None, "row", None, None, "col", None),)
    return jax.shard_map(
        on_device,
        mesh=mesh,
        in_specs=placed,
        out_specs=P(None, "row", None, None, "col", None),
        check_vma=False,
    )
```

```python
import jax
import jax.numpy as jnp
from jax import lax
from jax.sharding import PartitionSpec as P

STEPS = 3
HI = lax.Precision.HIGHEST


def mm_hi(a, b):
    return jnp.einsum(
        "...ps,qs->...pq", a, b, precision=HI, preferred_element_type=jnp.float32
    )


def mm_lo(a, b):
    return jnp.einsum(
        "...ps,qs->...pq",
        a.astype(jnp.bfloat16),
        b.astype(jnp.bfloat16),
        preferred_element_type=jnp.float32,
    )


def factor(tile, eye):
    half = tile.shape[0] // 2
    unit = eye[:half, :half]
    la = jnp.linalg.cholesky(tile[:half, :half])
    ia = lax.linalg.triangular_solve(la, unit, left_side=True, lower=True)
    lb = mm_hi(tile[half:, :half], ia)
    lc = jnp.linalg.cholesky(tile[half:, half:] - mm_hi(lb, lb))
    ic = lax.linalg.triangular_solve(lc, unit, left_side=True, lower=True)
    corner = -jnp.matmul(ic, jnp.matmul(lb, ia, precision=HI), precision=HI)
    zero = jnp.zeros_like(unit)
    low = jnp.block([[la, zero], [lb, lc]])
    inverse = jnp.block([[ia, zero], [corner, ic]])
    return low, inverse


def on_device(matrix):
    tile_rows = matrix.shape[0]
    width = matrix.shape[2]
    n_row = lax.axis_size("row")
    n_col = lax.axis_size("col")
    quarter = width // n_row
    my_row = lax.axis_index("row")
    my_col = lax.axis_index("col")
    tiles = matrix.reshape(tile_rows, width, width)
    eye = jnp.eye(width, dtype=jnp.float32)

    head = lax.all_gather(tiles[0], "row", axis=0, tiled=False)

    lane = width // 2
    rows = STEPS * width * 2 // n_col
    halves = head[:STEPS].reshape(STEPS * width, 2, lane)
    chunks = lax.all_to_all(halves.reshape(n_col, rows, lane), "col", 0, 0, tiled=True)
    lead = lax.all_gather(chunks[:STEPS], "col", axis=0, tiled=True)

    cols = lax.dynamic_slice_in_dim(head[:STEPS], my_row * quarter, quarter, axis=2)
    piece = jnp.swapaxes(cols, 1, 2)
    perm = []
    for c in range(n_col):
        for r in range(n_row):
            dst_col = c - c % n_row + r
            perm.append((c * n_row + r, dst_col * n_row + c % n_row))
    piece, lead = lax.optimization_barrier((piece, lead))
    piece = lax.ppermute(piece, ("col", "row"), perm)

    gathered = lax.all_gather(piece, "col", axis=1, tiled=False)
    raw = gathered.reshape(STEPS, tile_rows, width, width)

    lead = lead.reshape(n_col, STEPS, rows, lane)
    block = [lead[:, j].reshape(STEPS, width, width) for j in range(STEPS)]
    a00 = block[0][0]
    a10 = block[0][1]
    a20 = block[0][2]
    a11 = block[1][1]
    a21 = block[1][2]
    a22 = block[2][2]

    l0, i0 = factor(a00, eye)
    p01 = mm_hi(a10, i0)
    p02 = mm_hi(a20, i0)
    b11 = a11 - mm_hi(p01, p01)
    b21 = a21 - mm_hi(p02, p01)
    b22 = a22 - mm_hi(p02, p02)
    l1, i1 = factor(b11, eye)
    p12 = mm_hi(b21, i1)
    c22 = b22 - mm_hi(p12, p12)
    l2, i2 = factor(c22, eye)

    def sub(step, target, low_rows, partner, exact_rows):
        lo = mm_lo(low_rows, partner)
        hi = mm_hi(exact_rows, partner)
        t0 = my_row
        exact = (t0 == step) | (t0 == step + 1)
        first = jnp.where(exact, hi, lo[0])
        return target - lo.at[0].set(first)

    q0 = mm_hi(raw[0], i0)
    m1 = sub(1, raw[1], q0, p01, q0[0])
    q1 = mm_hi(m1, i1)
    m2 = sub(2, raw[2], q0, p02, q0[0])
    m2 = sub(2, m2, q1, p12, q1[0])
    q2 = mm_hi(m2, i2)

    own = jnp.swapaxes(head[:STEPS], 1, 2)
    c = my_col

    def own_sub(step, target, rows, partner):
        exact = (c == step) | (c == step + 1)
        return target - jnp.where(exact, mm_hi(rows, partner), mm_lo(rows, partner))

    r0 = mm_hi(own[0], i0)
    r1 = mm_hi(own_sub(1, own[1], r0, p01), i1)
    r2 = mm_hi(own_sub(2, own_sub(2, own[2], r0, p02), r1, p12), i2)

    update = mm_lo(q0, r0) + mm_lo(q1, r1) + mm_lo(q2, r2)
    offset = (my_row - c) % n_row
    near = c + offset
    local = jnp.clip((near - my_row) // n_row, 0, tile_rows - 1)
    valid = (offset <= 1) & (near < tile_rows * n_row)

    def row_of(q):
        return lax.dynamic_index_in_dim(q, local, 0, keepdims=False)

    exact = mm_hi(row_of(q0), r0) + mm_hi(row_of(q1), r1) + mm_hi(row_of(q2), r2)
    before = lax.dynamic_index_in_dim(update, local, 0, keepdims=False)
    chosen = jnp.where(valid, exact, before)
    update = lax.dynamic_update_index_in_dim(update, chosen, local, 0)

    row_ids = (jnp.arange(tile_rows, dtype=jnp.int32) * n_row + my_row)[:, None, None]
    trailing = jnp.where(row_ids >= c, tiles - update, tiles)
    panel = jnp.where(c == 0, q0, jnp.where(c == 1, q1, q2))
    diag = jnp.where(c == 0, l0, jnp.where(c == 1, l1, l2))
    leading = jnp.where(row_ids > c, panel, jnp.where(row_ids == c, diag[None], tiles))
    out = jnp.where(c >= STEPS, trailing, leading)
    return out.reshape(matrix.shape)


def solution(mesh):
    placed = (P(None, "row", None, None, "col", None),)
    return jax.shard_map(
        on_device,
        mesh=mesh,
        in_specs=placed,
        out_specs=P(None, "row", None, None, "col", None),
        check_vma=False,
    )
```

```python
import jax
import jax.numpy as jnp
from jax import lax
from jax.sharding import PartitionSpec as P

STEPS = 3
HI = lax.Precision.HIGH


def mm_hi(a, b):
    return jnp.einsum(
        "...ps,qs->...pq", a, b, precision=HI, preferred_element_type=jnp.float32
    )


def mm_lo(a, b):
    return jnp.einsum(
        "...ps,qs->...pq",
        a.astype(jnp.bfloat16),
        b.astype(jnp.bfloat16),
        preferred_element_type=jnp.float32,
    )


def factor(tile, eye):
    half = tile.shape[0] // 2
    unit = eye[:half, :half]
    la = jnp.linalg.cholesky(tile[:half, :half])
    ia = lax.linalg.triangular_solve(la, unit, left_side=True, lower=True)
    lb = mm_hi(tile[half:, :half], ia)
    lc = jnp.linalg.cholesky(tile[half:, half:] - mm_hi(lb, lb))
    ic = lax.linalg.triangular_solve(lc, unit, left_side=True, lower=True)
    corner = -jnp.matmul(ic, jnp.matmul(lb, ia, precision=HI), precision=HI)
    zero = jnp.zeros_like(unit)
    low = jnp.block([[la, zero], [lb, lc]])
    inverse = jnp.block([[ia, zero], [corner, ic]])
    return low, inverse


def on_device(matrix):
    tile_rows = matrix.shape[0]
    width = matrix.shape[2]
    n_row = lax.axis_size("row")
    n_col = lax.axis_size("col")
    quarter = width // n_row
    my_row = lax.axis_index("row")
    my_col = lax.axis_index("col")
    tiles = matrix.reshape(tile_rows, width, width)
    eye = jnp.eye(width, dtype=jnp.float32)

    head = lax.all_gather(tiles[0], "row", axis=0, tiled=False)

    rows = n_row * width // n_col
    chunks = lax.all_to_all(
        head.reshape(n_col, rows, width), "col", 0, 0, tiled=True
    )
    lead = lax.all_gather(chunks[:STEPS], "col", axis=0, tiled=True)

    cols = lax.dynamic_slice_in_dim(head[:STEPS], my_row * quarter, quarter, axis=2)
    piece = jnp.swapaxes(cols, 1, 2)
    perm = []
    for c in range(n_col):
        for r in range(n_row):
            dst_col = c - c % n_row + r
            perm.append((c * n_row + r, dst_col * n_row + c % n_row))
    piece, lead = lax.optimization_barrier((piece, lead))
    piece = lax.ppermute(piece, ("col", "row"), perm)

    gathered = lax.all_gather(piece, "col", axis=1, tiled=False)
    raw = gathered.reshape(STEPS, tile_rows, width, width)

    lead = lead.reshape(n_col, STEPS, rows, width)
    block = [lead[:, j].reshape(n_row, width, width) for j in range(STEPS)]
    a00 = block[0][0]
    a10 = block[0][1]
    a20 = block[0][2]
    a11 = block[1][1]
    a21 = block[1][2]
    a22 = block[2][2]

    l0, i0 = factor(a00, eye)
    p01 = mm_hi(a10, i0)
    p02 = mm_hi(a20, i0)
    b11 = a11 - mm_hi(p01, p01)
    b21 = a21 - mm_hi(p02, p01)
    b22 = a22 - mm_hi(p02, p02)
    l1, i1 = factor(b11, eye)
    p12 = mm_hi(b21, i1)
    c22 = b22 - mm_hi(p12, p12)
    l2, i2 = factor(c22, eye)

    def sub(step, target, low_rows, partner, exact_rows):
        lo = mm_lo(low_rows, partner)
        hi = mm_hi(exact_rows, partner)
        t0 = my_row
        exact = (t0 == step) | (t0 == step + 1)
        first = jnp.where(exact, hi, lo[0])
        return target - lo.at[0].set(first)

    q0 = mm_hi(raw[0], i0)
    m1 = sub(1, raw[1], q0, p01, q0[0])
    q1 = mm_hi(m1, i1)
    m2 = sub(2, raw[2], q0, p02, q0[0])
    m2 = sub(2, m2, q1, p12, q1[0])
    q2 = mm_hi(m2, i2)

    own = jnp.swapaxes(head[:STEPS], 1, 2)
    c = my_col

    def own_sub(step, target, rows, partner):
        exact = (c == step) | (c == step + 1)
        return target - jnp.where(exact, mm_hi(rows, partner), mm_lo(rows, partner))

    r0 = mm_hi(own[0], i0)
    r1 = mm_hi(own_sub(1, own[1], r0, p01), i1)
    r2 = mm_hi(own_sub(2, own_sub(2, own[2], r0, p02), r1, p12), i2)

    update = mm_lo(q0, r0) + mm_lo(q1, r1) + mm_lo(q2, r2)
    offset = (my_row - c) % n_row
    near = c + offset
    local = jnp.clip((near - my_row) // n_row, 0, tile_rows - 1)
    valid = (offset <= 1) & (near < tile_rows * n_row)

    def row_of(q):
        return lax.dynamic_index_in_dim(q, local, 0, keepdims=False)

    exact = mm_hi(row_of(q0), r0) + mm_hi(row_of(q1), r1) + mm_hi(row_of(q2), r2)
    before = lax.dynamic_index_in_dim(update, local, 0, keepdims=False)
    chosen = jnp.where(valid, exact, before)
    update = lax.dynamic_update_index_in_dim(update, chosen, local, 0)

    row_ids = (jnp.arange(tile_rows, dtype=jnp.int32) * n_row + my_row)[:, None, None]
    trailing = jnp.where(row_ids >= c, tiles - update, tiles)
    panel = jnp.where(c == 0, q0, jnp.where(c == 1, q1, q2))
    diag = jnp.where(c == 0, l0, jnp.where(c == 1, l1, l2))
    leading = jnp.where(row_ids > c, panel, jnp.where(row_ids == c, diag[None], tiles))
    out = jnp.where(c >= STEPS, trailing, leading)
    return out.reshape(matrix.shape)


def solution(mesh):
    placed = (P(None, "row", None, None, "col", None),)
    return jax.shard_map(
        on_device,
        mesh=mesh,
        in_specs=placed,
        out_specs=P(None, "row", None, None, "col", None),
        check_vma=False,
    )
```
